128 devices in a mesh: rows: 16 (over z, y), owners: 8 (over x, core).
Axes of the slice: x: 4, y: 4, z: 4, core: 2. Of those that a mesh axis runs over, the one named last changes fastest.
Arguments:
- instrument_feature_matrix: bfloat16 [131072, 1024], P(('rows', 'owners')), may hold values from -11 to 11
- partition_prototypes: float32 [1024, 1024], replicated, may hold values from -1.5 to 1.5
- softmax_sharpness_divisor: float32 [1], replicated, may hold values from 8 to 16
- chosen_partition_label: int32 [131072], P(('rows', 'owners')), may hold values from 0 to 1023, as said below
- partition_holder_team: int32 [1024], replicated, may hold values from 0 to 7, as said below
- orthogonal_quantizer_turn: bfloat16 [1024, 1024], replicated, may hold values from -0.1875 to 0.1875
Outputs:
- routed: bfloat16 [524288, 1024], P(('rows', 'owners'))
- new_centroids: float32 [1024, 1024], replicated
The draws below stay inside these ranges and needn't reach their ends.
Inputs may be any that keep to these rules, and one draw needn't show every extreme that they name: `partition_holder_team`: every owner group owns at least one cluster; the groups own unequal numbers of clusters. `chosen_partition_label`: among the rows of one device at most 512 have clusters of one owner group, and for every index along rows one owner group receives exactly 512 rows from each of the 8 devices of that index.
All inputs are finite; a program needn't handle non-finite values.
Results may differ from the reference program's by a relative error of at most 0.0035.
The reference program's roundings to bfloat16 on the way count: a program that leaves them out, or rounds other values in their place, can miss the bound.
Values may be sent and summed in bfloat16 or wider, within the bound.
No kernel may reach another device: no remote copies, remote signals or barrier semaphores. Data moves between devices by JAX's collectives and lax.ppermute only.
A program may use at most 128 MiB of HBM per device.

```python
import jax
import jax.numpy as jnp
from jax import lax

D = 1024
K = 1024
ROWS_DEV = 1024
CAP = 512
TOTAL_ROWS = 131072
N_ROWS = 16
N_OWNERS = 8


def shared_centroids(key):
    sub_key = jax.random.fold_in(key, 11)
    return jnp.clip(0.25 * jax.random.normal(sub_key, (K, D), jnp.float32), -1.5, 1.5)


def draw_partition_prototypes(key, part):
    return shared_centroids(key).astype(jnp.float32)


def draw_instrument_feature_matrix(key, part):
    sub_key = jax.random.fold_in(key, 13)
    key_two = jax.random.fold_in(sub_key, 1)
    values = jnp.clip(jax.random.normal(key_two, (TOTAL_ROWS, D), jnp.float32), -6.0, 6.0)
    return values.astype(jnp.bfloat16)


def owner_table(key):
    sub_key = jax.random.fold_in(key, 23)
    key_one, key_two, key_three, key_four = jax.random.split(sub_key, 4)
    first_draw = jax.random.randint(key_one, (K,), 0, N_OWNERS)
    second_draw = jax.random.randint(key_two, (K,), 0, N_OWNERS)
    unrotated_group = jnp.minimum(first_draw, second_draw)
    order = jax.random.permutation(key_three, K)
    unrotated_group = unrotated_group.at[order[:N_OWNERS]].set(jnp.arange(N_OWNERS, dtype=unrotated_group.dtype))
    labels = jax.random.permutation(key_four, N_OWNERS)
    return jnp.take(labels, unrotated_group).astype(jnp.int32)


def draw_partition_holder_team(key, part):
    return owner_table(key)


def draw_chosen_partition_label(key, part):
    table = owner_table(key)
    sub_key = jax.random.fold_in(key, 37)
    key_one, key_two, key_three, key_four = jax.random.split(sub_key, 4)
    devices_all = N_ROWS * N_OWNERS
    hot = jax.random.randint(key_one, (N_ROWS,), 0, N_OWNERS)
    hot_dev = jnp.repeat(hot, N_OWNERS)
    perms = jax.vmap(lambda one_key: jax.random.permutation(one_key, ROWS_DEV))(jax.random.split(key_two, devices_all))
    others = jax.random.randint(key_three, (devices_all, ROWS_DEV), 0, N_OWNERS - 1)
    target = jnp.where(perms < CAP, hot_dev[:, None], (hot_dev[:, None] + 1 + others) % N_OWNERS)
    order = jnp.argsort(table, stable=True)
    sizes = jnp.sum((table[:, None] == jnp.arange(N_OWNERS)[None, :]).astype(jnp.int32), axis=0)
    starts = jnp.cumsum(sizes) - sizes
    chooser = jax.random.randint(key_four, (devices_all, ROWS_DEV), 0, 1 << 20) % jnp.take(sizes, target)
    cluster = jnp.take(order, jnp.take(starts, target) + chooser)
    return cluster.reshape(-1).astype(jnp.int32)


def scatter_about(key, dims, spread, most, kind=jnp.bfloat16):
    values = jax.random.normal(key, dims, jnp.float32) * spread
    return jnp.minimum(jnp.maximum(values, -most), most).astype(kind)


def setup_inputs(seed: int = 0) -> dict:
    key_list = jax.random.split(jax.random.key(seed), 7)
    instrument_feature_matrix = draw_instrument_feature_matrix(jax.random.fold_in(key_list[6], 71), 0)
    partition_prototypes = draw_partition_prototypes(jax.random.fold_in(key_list[6], 71), 0)
    softmax_sharpness_divisor = jnp.clip(jax.random.uniform(key_list[2], (1,), jnp.float32, 8.0, 16.0), 8.0, 16.0)
    chosen_partition_label = draw_chosen_partition_label(jax.random.fold_in(key_list[6], 71), 0)
    partition_holder_team = draw_partition_holder_team(jax.random.fold_in(key_list[6], 71), 0)
    orthogonal_quantizer_turn = scatter_about(key_list[5], (D, D), D ** -0.5, 0.1875)
    return dict(instrument_feature_matrix=instrument_feature_matrix, partition_prototypes=partition_prototypes, softmax_sharpness_divisor=softmax_sharpness_divisor, chosen_partition_label=chosen_partition_label, partition_holder_team=partition_holder_team, orthogonal_quantizer_turn=orthogonal_quantizer_turn)


PRIOR = 32.0


def reference(instrument_feature_matrix, partition_prototypes, softmax_sharpness_divisor, chosen_partition_label, partition_holder_team, orthogonal_quantizer_turn):
    device_count = N_ROWS * N_OWNERS
    cent_bf = partition_prototypes.astype(jnp.bfloat16)
    prototype_length_squared_term = jnp.sum(partition_prototypes * partition_prototypes, axis=1)
    blocks = instrument_feature_matrix.reshape(device_count, ROWS_DEV, D)

    def accumulate(running, block_rows):
        part_sums, part_counts = running
        pairwise_dot_matrix = jnp.dot(block_rows, cent_bf.T, preferred_element_type=jnp.float32)
        partition_affinity_logits = (2.0 * pairwise_dot_matrix - prototype_length_squared_term[None, :]) / softmax_sharpness_divisor[0]
        weights = jax.nn.softmax(partition_affinity_logits, axis=1)
        weights_bf = weights.astype(jnp.bfloat16)
        part_sums = part_sums + jnp.dot(weights_bf.T, block_rows, preferred_element_type=jnp.float32)
        part_counts = part_counts + jnp.sum(weights, axis=0)
        return (part_sums, part_counts), None

    start_state = (jnp.zeros((K, D), jnp.float32), jnp.zeros((K,), jnp.float32))
    (total_sums, total_counts), _ = lax.scan(accumulate, start_state, blocks)
    new_centroids = (total_sums + PRIOR * partition_prototypes) / (total_counts + PRIOR)[:, None]
    picked = jnp.take(new_centroids, chosen_partition_label, axis=0)
    residual_vectors = (instrument_feature_matrix.astype(jnp.float32) - picked).astype(jnp.bfloat16)
    rotated = jnp.dot(residual_vectors, orthogonal_quantizer_turn, preferred_element_type=jnp.float32).astype(jnp.bfloat16)
    owner_group = jnp.take(partition_holder_team, chosen_partition_label, axis=0).reshape(device_count, ROWS_DEV)
    onehot = (owner_group[:, :, None] == jnp.arange(N_OWNERS, dtype=jnp.int32)[None, None, :]).astype(jnp.int32)
    before = jnp.cumsum(onehot, axis=1) - onehot
    rank_in_group = jnp.sum(before * onehot, axis=2)
    device_ids = jnp.arange(device_count, dtype=jnp.int32)[:, None]
    row_shard = device_ids // N_OWNERS
    source = device_ids % N_OWNERS
    target = ((row_shard * N_OWNERS + owner_group) * N_OWNERS + source) * CAP + rank_in_group
    routed = jnp.zeros((device_count * N_OWNERS * CAP, D), jnp.bfloat16)
    routed = routed.at[target.reshape(-1).astype(jnp.int32)].set(rotated)
    return routed, new_centroids
```

```python
import jax
import jax.numpy as jnp
from jax import lax
from jax.sharding import PartitionSpec as P

CAP = 512


PRIOR = 32.0


def shards(
    instrument_feature_matrix,
    partition_prototypes,
    softmax_sharpness_divisor,
    chosen_partition_label,
    partition_holder_team,
    orthogonal_quantizer_turn,
):
    groups = lax.axis_size("owners")
    clusters, width = partition_prototypes.shape
    rows = instrument_feature_matrix.shape[0]
    x = instrument_feature_matrix
    labels = chosen_partition_label

    cent_bf = partition_prototypes.astype(jnp.bfloat16)
    prototype_length_squared_term = jnp.sum(partition_prototypes * partition_prototypes, axis=1)
    pairwise_dot_matrix = jnp.dot(x, cent_bf.T, preferred_element_type=jnp.float32)
    partition_affinity_logits = (
        2.0 * pairwise_dot_matrix - prototype_length_squared_term[None, :]
    ) / softmax_sharpness_divisor[0]
    weights = jax.nn.softmax(partition_affinity_logits, axis=1)
    weights_bf = weights.astype(jnp.bfloat16)
    part_sums = jnp.dot(weights_bf.T, x, preferred_element_type=jnp.float32)
    part_counts = jnp.sum(weights, axis=0)
    pad = (-(clusters + 1)) % 8
    packed = jnp.concatenate(
        [part_sums, part_counts.reshape(1, width), jnp.zeros((pad, width), jnp.float32)], axis=0
    )
    total = lax.psum(packed, ("rows", "owners"))

    owner_group = jnp.take(partition_holder_team, labels, axis=0)
    onehot = (owner_group[:, None] == jnp.arange(groups, dtype=jnp.int32)[None, :]).astype(jnp.int32)
    before = jnp.cumsum(onehot, axis=0) - onehot
    rank_in_group = jnp.sum(before * onehot, axis=1)
    slot_index = owner_group * CAP + rank_in_group
    source_row = (
        jnp.full((groups * CAP,), -1, jnp.int32).at[slot_index].set(jnp.arange(rows, dtype=jnp.int32))
    )
    filled = source_row >= 0
    safe_row = jnp.where(filled, source_row, 0)
    slot_x = jnp.take(x, safe_row, axis=0)
    slot_label = jnp.where(filled, jnp.take(labels, safe_row, axis=0), -1)
    recv_x = lax.all_to_all(
        slot_x.reshape(groups, CAP, width), "owners", split_axis=0, concat_axis=0, tiled=True
    ).reshape(groups * CAP, width)
    recv_label = lax.all_to_all(
        slot_label.reshape(groups, CAP), "owners", split_axis=0, concat_axis=0, tiled=True
    ).reshape(groups * CAP)

    total_sums = total[:clusters]
    total_counts = total[clusters]
    new_centroids = (total_sums + PRIOR * partition_prototypes) / (total_counts + PRIOR)[:, None]

    valid = recv_label >= 0
    picked = jnp.take(new_centroids, jnp.where(valid, recv_label, 0), axis=0)
    residual_vectors = (recv_x.astype(jnp.float32) - picked).astype(jnp.bfloat16)
    rotated = jnp.dot(
        residual_vectors, orthogonal_quantizer_turn, preferred_element_type=jnp.float32
    ).astype(jnp.bfloat16)
    routed = jnp.where(valid[:, None], rotated, jnp.zeros_like(rotated))
    return (routed, new_centroids)


def solution(mesh):
    return jax.shard_map(
        shards,
        mesh=mesh,
        in_specs=(P(("rows", "owners"), None), P(), P(), P(("rows", "owners")), P(), P()),
        out_specs=(P(("rows", "owners"), None), P()),
        check_vma=False,
    )
```

```python
import jax
import jax.numpy as jnp
from jax import lax
from jax.sharding import PartitionSpec as P

CAP = 512


PRIOR = 32.0


def shards(
    instrument_feature_matrix,
    partition_prototypes,
    softmax_sharpness_divisor,
    chosen_partition_label,
    partition_holder_team,
    orthogonal_quantizer_turn,
):
    groups = lax.axis_size("owners")
    clusters, width = partition_prototypes.shape
    rows = instrument_feature_matrix.shape[0]
    x = instrument_feature_matrix
    labels = chosen_partition_label

    cent_bf = partition_prototypes.astype(jnp.bfloat16)
    prototype_length_squared_term = jnp.sum(partition_prototypes * partition_prototypes, axis=1)
    pairwise_dot_matrix = jnp.dot(x, cent_bf.T, preferred_element_type=jnp.float32)
    partition_affinity_logits = (
        2.0 * pairwise_dot_matrix - prototype_length_squared_term[None, :]
    ) / softmax_sharpness_divisor[0]
    weights = jax.nn.softmax(partition_affinity_logits, axis=1)
    weights_bf = weights.astype(jnp.bfloat16)
    part_sums = jnp.dot(weights_bf.T, x, preferred_element_type=jnp.float32)
    part_counts = jnp.sum(weights, axis=0)
    pad = (-(clusters + 1)) % 8
    packed = jnp.concatenate(
        [part_sums, part_counts.reshape(1, width), jnp.zeros((pad, width), jnp.float32)], axis=0
    )
    total = lax.psum(packed, ("rows", "owners"))
    packed, x, labels = lax.optimization_barrier((packed, x, labels))

    owner_group = jnp.take(partition_holder_team, labels, axis=0, mode="clip")
    onehot = (owner_group[:, None] == jnp.arange(groups, dtype=jnp.int32)[None, :]).astype(jnp.int32)
    before = jnp.cumsum(onehot, axis=0) - onehot
    rank_in_group = jnp.sum(before * onehot, axis=1)
    slot_index = owner_group * CAP + rank_in_group
    source_row = (
        jnp.zeros((groups * CAP,), jnp.int32).at[slot_index].set(jnp.arange(rows, dtype=jnp.int32))
    )
    slot_label = jnp.full((groups * CAP,), -1, jnp.int32).at[slot_index].set(labels)
    slot_x = jnp.take(x, source_row, axis=0, mode="clip")
    recv_x = lax.all_to_all(
        slot_x.reshape(groups, CAP, width), "owners", split_axis=0, concat_axis=0, tiled=True
    ).reshape(groups * CAP, width)
    recv_label = lax.all_to_all(
        slot_label.reshape(groups, CAP), "owners", split_axis=0, concat_axis=0, tiled=True
    ).reshape(groups * CAP)

    total_sums = total[:clusters]
    total_counts = total[clusters]
    new_centroids = (total_sums + PRIOR * partition_prototypes) / (total_counts + PRIOR)[:, None]

    valid = recv_label >= 0
    picked = jnp.take(new_centroids, recv_label, axis=0, mode="clip")
    residual_vectors = (recv_x.astype(jnp.float32) - picked).astype(jnp.bfloat16)
    rotated = jnp.dot(
        residual_vectors, orthogonal_quantizer_turn, preferred_element_type=jnp.float32
    ).astype(jnp.bfloat16)
    routed = jnp.where(valid[:, None], rotated, jnp.zeros_like(rotated))
    return (routed, new_centroids)


def solution(mesh):
    return jax.shard_map(
        shards,
        mesh=mesh,
        in_specs=(P(("rows", "owners"), None), P(), P(), P(("rows", "owners")), P(), P()),
        out_specs=(P(("rows", "owners"), None), P()),
        check_vma=False,
    )
```

```python
import jax
import jax.numpy as jnp
from jax import lax
from jax.sharding import PartitionSpec as P

CAP = 512


PRIOR = 32.0


def shards(
    instrument_feature_matrix,
    partition_prototypes,
    softmax_sharpness_divisor,
    chosen_partition_label,
    partition_holder_team,
    orthogonal_quantizer_turn,
):
    groups = lax.axis_size("owners")
    clusters, width = partition_prototypes.shape
    rows = instrument_feature_matrix.shape[0]
    x = instrument_feature_matrix
    labels = chosen_partition_label

    cent_bf = partition_prototypes.astype(jnp.bfloat16)
    prototype_length_squared_term = jnp.sum(partition_prototypes * partition_prototypes, axis=1)
    pairwise_dot_matrix = jnp.dot(x, cent_bf.T, preferred_element_type=jnp.float32)
    partition_affinity_logits = (
        2.0 * pairwise_dot_matrix - prototype_length_squared_term[None, :]
    ) / softmax_sharpness_divisor[0]
    weights = jax.nn.softmax(partition_affinity_logits, axis=1)
    weights_bf = weights.astype(jnp.bfloat16)
    part_counts = jnp.sum(weights, axis=0)
    pad = 8
    weights_wide = jnp.pad(weights_bf, ((0, 0), (0, pad)))
    packed = lax.dot_general(
        weights_wide, x, (((0,), (0,)), ((), ())), preferred_element_type=jnp.float32
    )
    packed = lax.dynamic_update_slice(packed, part_counts.reshape(1, width), (clusters, 0))
    total = lax.psum(packed, ("rows", "owners"))
    packed, x, labels = lax.optimization_barrier((packed, x, labels))

    owner_group = jnp.take(partition_holder_team, labels, axis=0, mode="clip")
    onehot = (owner_group[:, None] == jnp.arange(groups, dtype=jnp.int32)[None, :]).astype(jnp.int32)
    before = jnp.cumsum(onehot, axis=0) - onehot
    rank_in_group = jnp.sum(before * onehot, axis=1)
    slot_index = owner_group * CAP + rank_in_group
    source_row = (
        jnp.zeros((groups * CAP,), jnp.int32).at[slot_index].set(jnp.arange(rows, dtype=jnp.int32))
    )
    slot_label = jnp.full((groups * CAP,), -1, jnp.int32).at[slot_index].set(labels)
    slot_x = jnp.take(x, source_row, axis=0, mode="clip")
    recv_x = lax.all_to_all(
        slot_x.reshape(groups, CAP, width), "owners", split_axis=0, concat_axis=0, tiled=True
    ).reshape(groups * CAP, width)
    recv_label = lax.all_to_all(
        slot_label.reshape(groups, CAP), "owners", split_axis=0, concat_axis=0, tiled=True
    ).reshape(groups * CAP)

    total_sums = total[:clusters]
    total_counts = total[clusters]
    new_centroids = (total_sums + PRIOR * partition_prototypes) / (total_counts + PRIOR)[:, None]

    valid = recv_label >= 0
    picked = jnp.take(new_centroids, recv_label, axis=0, mode="clip")
    residual_vectors = (recv_x.astype(jnp.float32) - picked).astype(jnp.bfloat16)
    residual_vectors = jnp.where(valid[:, None], residual_vectors, jnp.zeros_like(residual_vectors))
    residual_vectors = lax.optimization_barrier(residual_vectors)
    routed = jnp.dot(
        residual_vectors, orthogonal_quantizer_turn, preferred_element_type=jnp.float32
    ).astype(jnp.bfloat16)
    return (routed, new_centroids)


def solution(mesh):
    return jax.shard_map(
        shards,
        mesh=mesh,
        in_specs=(P(("rows", "owners"), None), P(), P(), P(("rows", "owners")), P(), P()),
        out_specs=(P(("rows", "owners"), None), P()),
        check_vma=False,
    )
```

```python
import jax
import jax.numpy as jnp
from jax import lax
from jax.sharding import PartitionSpec as P

CAP = 512


PRIOR = 32.0


def shards(
    instrument_feature_matrix,
    partition_prototypes,
    softmax_sharpness_divisor,
    chosen_partition_label,
    partition_holder_team,
    orthogonal_quantizer_turn,
):
    groups = lax.axis_size("owners")
    clusters, width = partition_prototypes.shape
    rows = instrument_feature_matrix.shape[0]
    x = instrument_feature_matrix
    labels = chosen_partition_label

    cent_bf = partition_prototypes.astype(jnp.bfloat16)
    prototype_length_squared_term = jnp.sum(partition_prototypes * partition_prototypes, axis=1)
    pairwise_dot_matrix = jnp.dot(x, cent_bf.T, preferred_element_type=jnp.float32)
    partition_affinity_logits = (
        2.0 * pairwise_dot_matrix - prototype_length_squared_term[None, :]
    ) / softmax_sharpness_divisor[0]
    weights = jax.nn.softmax(partition_affinity_logits, axis=1)
    weights_bf = weights.astype(jnp.bfloat16)
    part_counts = jnp.sum(weights, axis=0)
    pad = 8
    weights_wide = jnp.pad(weights_bf, ((0, 0), (0, pad)))
    packed = lax.dot_general(
        weights_wide, x, (((0,), (0,)), ((), ())), preferred_element_type=jnp.float32
    )
    packed = lax.dynamic_update_slice(packed, part_counts.reshape(1, width), (clusters, 0))
    total = lax.psum(packed, ("rows", "owners"))
    packed, x, labels = lax.optimization_barrier((packed, x, labels))

    owner_group = jnp.take(partition_holder_team, labels, axis=0, mode="clip")
    onehot = (owner_group[:, None] == jnp.arange(groups, dtype=jnp.int32)[None, :]).astype(jnp.int32)
    before = jnp.cumsum(onehot, axis=0) - onehot
    rank_in_group = jnp.sum(before * onehot, axis=1)
    slot_index = owner_group * CAP + rank_in_group
    source_row = (
        jnp.zeros((groups * CAP,), jnp.int32).at[slot_index].set(jnp.arange(rows, dtype=jnp.int32))
    )
    slot_label = jnp.full((groups * CAP,), -1, jnp.int32).at[slot_index].set(labels)
    slot_x = jnp.take(x, source_row, axis=0, mode="clip")
    recv_x = lax.all_to_all(
        slot_x.reshape(groups, CAP, width), "owners", split_axis=0, concat_axis=0, tiled=True
    ).reshape(groups * CAP, width)
    recv_label = lax.all_to_all(
        slot_label.reshape(groups, CAP), "owners", split_axis=0, concat_axis=0, tiled=True
    ).reshape(groups * CAP)

    valid = recv_label >= 0
    chooser = (recv_label[:, None] == jnp.arange(clusters, dtype=jnp.int32)[None, :]).astype(
        jnp.bfloat16
    )
    chooser = jnp.concatenate([chooser, chooser], axis=1)

    total_sums = total[:clusters]
    total_counts = total[clusters]
    new_centroids = (total_sums + PRIOR * partition_prototypes) * (
        1.0 / (total_counts + PRIOR)
    )[:, None]
    high = new_centroids.astype(jnp.bfloat16)
    low = (new_centroids - high.astype(jnp.float32)).astype(jnp.bfloat16)
    picked = jnp.dot(
        chooser, jnp.concatenate([high, low], axis=0), preferred_element_type=jnp.float32
    )
    residual_vectors = (recv_x.astype(jnp.float32) - picked).astype(jnp.bfloat16)
    residual_vectors = jnp.where(valid[:, None], residual_vectors, jnp.zeros_like(residual_vectors))
    routed = jnp.dot(
        residual_vectors, orthogonal_quantizer_turn, preferred_element_type=jnp.float32
    ).astype(jnp.bfloat16)
    return (routed, new_centroids)


def solution(mesh):
    return jax.shard_map(
        shards,
        mesh=mesh,
        in_specs=(P(("rows", "owners"), None), P(), P(), P(("rows", "owners")), P(), P()),
        out_specs=(P(("rows", "owners"), None), P()),
        check_vma=False,
    )
```

```python
import jax
import jax.numpy as jnp
from jax import lax
from jax.sharding import PartitionSpec as P

CAP = 512


PRIOR = 32.0


def shards(
    instrument_feature_matrix,
    partition_prototypes,
    softmax_sharpness_divisor,
    chosen_partition_label,
    partition_holder_team,
    orthogonal_quantizer_turn,
):
    groups = lax.axis_size("owners")
    clusters, width = partition_prototypes.shape
    rows = instrument_feature_matrix.shape[0]
    x = instrument_feature_matrix
    labels = chosen_partition_label

    cent_bf = partition_prototypes.astype(jnp.bfloat16)
    prototype_length_squared_term = jnp.sum(partition_prototypes * partition_prototypes, axis=1)
    pairwise_dot_matrix = jnp.dot(x, cent_bf.T, preferred_element_type=jnp.float32)
    partition_affinity_logits = (
        2.0 * pairwise_dot_matrix - prototype_length_squared_term[None, :]
    ) / softmax_sharpness_divisor[0]
    weights = jax.nn.softmax(partition_affinity_logits, axis=1)
    weights_bf = weights.astype(jnp.bfloat16)
    part_counts = jnp.sum(weights, axis=0)
    pad = 8
    weights_wide = jnp.pad(weights_bf, ((0, 0), (0, pad)))
    packed = lax.dot_general(
        weights_wide, x, (((0,), (0,)), ((), ())), preferred_element_type=jnp.float32
    )
    packed = lax.dynamic_update_slice(packed, part_counts.reshape(1, width), (clusters, 0))
    total = lax.psum(packed, ("rows", "owners"))
    packed, x, labels = lax.optimization_barrier((packed, x, labels))

    owner_group = jnp.take(partition_holder_team, labels, axis=0, mode="clip")
    onehot = (owner_group[:, None] == jnp.arange(groups, dtype=jnp.int32)[None, :]).astype(jnp.int32)
    before = jnp.cumsum(onehot, axis=0) - onehot
    rank_in_group = jnp.sum(before * onehot, axis=1)
    slot_index = owner_group * CAP + rank_in_group
    source_row = (
        jnp.zeros((groups * CAP,), jnp.int32).at[slot_index].set(jnp.arange(rows, dtype=jnp.int32))
    )
    slot_label = jnp.full((groups * CAP,), -1, jnp.int32).at[slot_index].set(labels)
    slot_x = jnp.take(x, source_row, axis=0, mode="clip")
    recv_x = lax.all_to_all(
        slot_x.reshape(groups, CAP, width), "owners", split_axis=0, concat_axis=0, tiled=True
    ).reshape(groups * CAP, width)
    recv_label = lax.all_to_all(
        slot_label.reshape(groups, CAP), "owners", split_axis=0, concat_axis=0, tiled=True
    ).reshape(groups * CAP)

    valid = recv_label >= 0
    chooser = (recv_label[:, None] == jnp.arange(clusters, dtype=jnp.int32)[None, :]).astype(
        jnp.bfloat16
    )
    chooser = jnp.concatenate([chooser, chooser], axis=1)

    total_sums = total[:clusters]
    total_counts = total[clusters]
    new_centroids = (total_sums + PRIOR * partition_prototypes) * (
        1.0 / (total_counts + PRIOR)
    )[:, None]
    high = lax.reduce_precision(new_centroids, exponent_bits=8, mantissa_bits=7)
    low = (new_centroids - high).astype(jnp.bfloat16)
    picked = jnp.dot(
        chooser,
        jnp.concatenate([high.astype(jnp.bfloat16), low], axis=0),
        preferred_element_type=jnp.float32,
    )
    residual_vectors = (recv_x.astype(jnp.float32) - picked).astype(jnp.bfloat16)
    residual_vectors = jnp.where(valid[:, None], residual_vectors, jnp.zeros_like(residual_vectors))
    routed = jnp.dot(
        residual_vectors, orthogonal_quantizer_turn, preferred_element_type=jnp.float32
    ).astype(jnp.bfloat16)
    return (routed, new_centroids)


def solution(mesh):
    return jax.shard_map(
        shards,
        mesh=mesh,
        in_specs=(P(("rows", "owners"), None), P(), P(), P(("rows", "owners")), P(), P()),
        out_specs=(P(("rows", "owners"), None), P()),
        check_vma=False,
    )
```

```python
import jax
import jax.numpy as jnp
from jax import lax
from jax.sharding import PartitionSpec as P

CAP = 512


PRIOR = 32.0


def _ring(axis, shift):
    if axis == "y":
        return "rows", [(z * 4 + y, z * 4 + (y + shift) % 4) for z in range(4) for y in range(4)]
    if axis == "z":
        return "rows", [(z * 4 + y, ((z + shift) % 4) * 4 + y) for z in range(4) for y in range(4)]
    return "owners", [(x * 2 + c, ((x + shift) % 4) * 2 + c) for x in range(4) for c in range(2)]


def _place(axis):
    if axis == "y":
        return lax.axis_index("rows") % 4
    if axis == "z":
        return lax.axis_index("rows") // 4
    return lax.axis_index("owners") // 2


_CORES = [(s, s ^ 1) for s in range(8)]


def _scatter_sum(d, axis):
    if axis == "core":
        me = lax.axis_index("owners") % 2
        halves = d.reshape(2, d.shape[0] // 2, d.shape[1])
        mine = lax.dynamic_index_in_dim(halves, me, 0, keepdims=False)
        other = lax.dynamic_index_in_dim(halves, 1 - me, 0, keepdims=False)
        return mine + lax.ppermute(other, "owners", _CORES)
    me = _place(axis)
    pieces = d.reshape(4, d.shape[0] // 4, d.shape[1])
    acc = lax.dynamic_index_in_dim(pieces, me, 0, keepdims=False)
    for shift in (1, 2, 3):
        name, perm = _ring(axis, shift)
        piece = lax.dynamic_index_in_dim(pieces, (me + shift) % 4, 0, keepdims=False)
        acc = acc + lax.ppermute(piece, name, perm)
    return acc


def _gather(d, axis):
    if axis == "core":
        me = lax.axis_index("owners") % 2
        out = jnp.zeros((2,) + d.shape, d.dtype)
        out = lax.dynamic_update_index_in_dim(out, d, me, 0)
        out = lax.dynamic_update_index_in_dim(out, lax.ppermute(d, "owners", _CORES), 1 - me, 0)
        return out.reshape(2 * d.shape[0], d.shape[1])
    me = _place(axis)
    out = jnp.zeros((4,) + d.shape, d.dtype)
    out = lax.dynamic_update_index_in_dim(out, d, me, 0)
    for shift in (1, 2, 3):
        name, perm = _ring(axis, shift)
        out = lax.dynamic_update_index_in_dim(out, lax.ppermute(d, name, perm), (me - shift) % 4, 0)
    return out.reshape(4 * d.shape[0], d.shape[1])


def _all_sum(d):
    order = ("core", "y", "z", "x")
    for axis in order:
        d = _scatter_sum(d, axis)
    for axis in reversed(order):
        d = _gather(d, axis)
    return d


def shards(
    instrument_feature_matrix,
    partition_prototypes,
    softmax_sharpness_divisor,
    chosen_partition_label,
    partition_holder_team,
    orthogonal_quantizer_turn,
):
    groups = lax.axis_size("owners")
    clusters, width = partition_prototypes.shape
    rows = instrument_feature_matrix.shape[0]
    x = instrument_feature_matrix
    labels = chosen_partition_label

    cent_bf = partition_prototypes.astype(jnp.bfloat16)
    prototype_length_squared_term = jnp.sum(partition_prototypes * partition_prototypes, axis=1)
    pairwise_dot_matrix = jnp.dot(x, cent_bf.T, preferred_element_type=jnp.float32)
    partition_affinity_logits = (
        2.0 * pairwise_dot_matrix - prototype_length_squared_term[None, :]
    ) / softmax_sharpness_divisor[0]
    weights = jax.nn.softmax(partition_affinity_logits, axis=1)
    weights_bf = weights.astype(jnp.bfloat16)
    part_counts = jnp.sum(weights, axis=0)
    pad = (-(clusters + 1)) % 128 + 1
    weights_wide = jnp.pad(weights_bf, ((0, 0), (0, pad)))
    packed = lax.dot_general(
        weights_wide, x, (((0,), (0,)), ((), ())), preferred_element_type=jnp.float32
    )
    packed = lax.dynamic_update_slice(packed, part_counts.reshape(1, width), (clusters, 0))
    total = _all_sum(packed)
    packed, x, labels = lax.optimization_barrier((packed, x, labels))

    owner_group = jnp.take(partition_holder_team, labels, axis=0, mode="clip")
    onehot = (owner_group[:, None] == jnp.arange(groups, dtype=jnp.int32)[None, :]).astype(jnp.int32)
    before = jnp.cumsum(onehot, axis=0) - onehot
    rank_in_group = jnp.sum(before * onehot, axis=1)
    slot_index = owner_group * CAP + rank_in_group
    source_row = (
        jnp.zeros((groups * CAP,), jnp.int32).at[slot_index].set(jnp.arange(rows, dtype=jnp.int32))
    )
    slot_label = jnp.full((groups * CAP,), -1, jnp.int32).at[slot_index].set(labels)
    slot_x = jnp.take(x, source_row, axis=0, mode="clip")
    recv_x = lax.all_to_all(
        slot_x.reshape(groups, CAP, width), "owners", split_axis=0, concat_axis=0, tiled=True
    ).reshape(groups * CAP, width)
    recv_label = lax.all_to_all(
        slot_label.reshape(groups, CAP), "owners", split_axis=0, concat_axis=0, tiled=True
    ).reshape(groups * CAP)

    valid = recv_label >= 0
    chooser = (recv_label[:, None] == jnp.arange(clusters, dtype=jnp.int32)[None, :]).astype(
        jnp.bfloat16
    )
    chooser = jnp.concatenate([chooser, chooser], axis=1)

    total_sums = total[:clusters]
    total_counts = total[clusters]
    new_centroids = (total_sums + PRIOR * partition_prototypes) * (
        1.0 / (total_counts + PRIOR)
    )[:, None]
    high = lax.reduce_precision(new_centroids, exponent_bits=8, mantissa_bits=7)
    low = (new_centroids - high).astype(jnp.bfloat16)
    picked = jnp.dot(
        chooser,
        jnp.concatenate([high.astype(jnp.bfloat16), low], axis=0),
        preferred_element_type=jnp.float32,
    )
    residual_vectors = (recv_x.astype(jnp.float32) - picked).astype(jnp.bfloat16)
    residual_vectors = jnp.where(valid[:, None], residual_vectors, jnp.zeros_like(residual_vectors))
    routed = jnp.dot(
        residual_vectors, orthogonal_quantizer_turn, preferred_element_type=jnp.float32
    ).astype(jnp.bfloat16)
    return (routed, new_centroids)


def solution(mesh):
    return jax.shard_map(
        shards,
        mesh=mesh,
        in_specs=(P(("rows", "owners"), None), P(), P(), P(("rows", "owners")), P(), P()),
        out_specs=(P(("rows", "owners"), None), P()),
        check_vma=False,
    )
```

```python
import jax
import jax.numpy as jnp
from jax import lax
from jax.sharding import PartitionSpec as P

CAP = 512


PRIOR = 32.0


def _ring(axis, shift):
    if axis == "y":
        return "rows", [(z * 4 + y, z * 4 + (y + shift) % 4) for z in range(4) for y in range(4)]
    if axis == "z":
        return "rows", [(z * 4 + y, ((z + shift) % 4) * 4 + y) for z in range(4) for y in range(4)]
    return "owners", [(x * 2 + c, ((x + shift) % 4) * 2 + c) for x in range(4) for c in range(2)]


def _place(axis):
    if axis == "y":
        return lax.axis_index("rows") % 4
    if axis == "z":
        return lax.axis_index("rows") // 4
    return lax.axis_index("owners") // 2


_CORES = [(s, s ^ 1) for s in range(8)]


def _scatter_sum(d, axis):
    if axis == "core":
        me = lax.axis_index("owners") % 2
        halves = d.reshape(2, d.shape[0] // 2, d.shape[1])
        mine = lax.dynamic_index_in_dim(halves, me, 0, keepdims=False)
        other = lax.dynamic_index_in_dim(halves, 1 - me, 0, keepdims=False)
        return mine + lax.ppermute(other, "owners", _CORES)
    me = _place(axis)
    pieces = d.reshape(4, d.shape[0] // 4, d.shape[1])
    acc = lax.dynamic_index_in_dim(pieces, me, 0, keepdims=False)
    for shift in (1, 2, 3):
        name, perm = _ring(axis, shift)
        piece = lax.dynamic_index_in_dim(pieces, (me + shift) % 4, 0, keepdims=False)
        acc = acc + lax.ppermute(piece, name, perm)
    return acc


def _gather(d, axis):
    if axis == "core":
        me = lax.axis_index("owners") % 2
        out = jnp.zeros((2,) + d.shape, d.dtype)
        out = lax.dynamic_update_index_in_dim(out, d, me, 0)
        out = lax.dynamic_update_index_in_dim(out, lax.ppermute(d, "owners", _CORES), 1 - me, 0)
        return out.reshape(2 * d.shape[0], d.shape[1])
    me = _place(axis)
    out = jnp.zeros((4,) + d.shape, d.dtype)
    out = lax.dynamic_update_index_in_dim(out, d, me, 0)
    for shift in (1, 2, 3):
        name, perm = _ring(axis, shift)
        out = lax.dynamic_update_index_in_dim(out, lax.ppermute(d, name, perm), (me - shift) % 4, 0)
    return out.reshape(4 * d.shape[0], d.shape[1])


def _all_sum(d):
    order = ("core", "y", "z", "x")
    for axis in order:
        d = _scatter_sum(d, axis)
    for axis in reversed(order):
        d = _gather(d, axis)
    return d


def shards(
    instrument_feature_matrix,
    partition_prototypes,
    softmax_sharpness_divisor,
    chosen_partition_label,
    partition_holder_team,
    orthogonal_quantizer_turn,
):
    groups = lax.axis_size("owners")
    clusters, width = partition_prototypes.shape
    rows = instrument_feature_matrix.shape[0]
    x = instrument_feature_matrix
    labels = chosen_partition_label

    cent_bf = partition_prototypes.astype(jnp.bfloat16)
    prototype_length_squared_term = jnp.sum(partition_prototypes * partition_prototypes, axis=1)
    pairwise_dot_matrix = jnp.dot(x, cent_bf.T, preferred_element_type=jnp.float32)
    partition_affinity_logits = (
        2.0 * pairwise_dot_matrix - prototype_length_squared_term[None, :]
    ) / softmax_sharpness_divisor[0]
    weights = jax.nn.softmax(partition_affinity_logits, axis=1)
    weights_bf = weights.astype(jnp.bfloat16)
    part_counts = jnp.sum(weights, axis=0)
    pad = (-(clusters + 1)) % 128 + 1
    weights_wide = jnp.pad(weights_bf, ((0, 0), (0, pad)))
    packed = lax.dot_general(
        weights_wide, x, (((0,), (0,)), ((), ())), preferred_element_type=jnp.float32
    )
    packed = lax.dynamic_update_slice(packed, part_counts.reshape(1, width), (clusters, 0))
    partial = packed
    for axis in ("core", "y", "z"):
        partial = _scatter_sum(partial, axis)

    owner_group = jnp.take(partition_holder_team, labels, axis=0, mode="clip")
    onehot = (owner_group[:, None] == jnp.arange(groups, dtype=jnp.int32)[None, :]).astype(jnp.int32)
    before = jnp.cumsum(onehot, axis=0) - onehot
    rank_in_group = jnp.sum(before * onehot, axis=1)
    slot_index = owner_group * CAP + rank_in_group
    source_row = (
        jnp.zeros((groups * CAP,), jnp.int32).at[slot_index].set(jnp.arange(rows, dtype=jnp.int32))
    )
    slot_label = jnp.full((groups * CAP,), -1, jnp.int32).at[slot_index].set(labels)
    slot_x = jnp.take(x, source_row, axis=0, mode="clip")
    slot_x = slot_x.reshape(groups, CAP, width)
    half = CAP // 2
    recv_first = lax.all_to_all(slot_x[:, :half], "owners", split_axis=0, concat_axis=0, tiled=True)
    partial, recv_first = lax.optimization_barrier((partial, recv_first))
    partial = _scatter_sum(partial, "x")
    partial = _gather(partial, "x")
    partial, second = lax.optimization_barrier((partial, slot_x[:, half:]))
    recv_second = lax.all_to_all(second, "owners", split_axis=0, concat_axis=0, tiled=True)
    for axis in ("z", "y", "core"):
        partial = _gather(partial, axis)
    total = partial
    recv_x = jnp.concatenate([recv_first, recv_second], axis=1).reshape(groups * CAP, width)
    recv_label = lax.all_to_all(
        slot_label.reshape(groups, CAP), "owners", split_axis=0, concat_axis=0, tiled=True
    ).reshape(groups * CAP)

    valid = recv_label >= 0
    chooser = (recv_label[:, None] == jnp.arange(clusters, dtype=jnp.int32)[None, :]).astype(
        jnp.bfloat16
    )
    chooser = jnp.concatenate([chooser, chooser], axis=1)

    total_sums = total[:clusters]
    total_counts = total[clusters]
    new_centroids = (total_sums + PRIOR * partition_prototypes) * (
        1.0 / (total_counts + PRIOR)
    )[:, None]
    high = lax.reduce_precision(new_centroids, exponent_bits=8, mantissa_bits=7)
    low = (new_centroids - high).astype(jnp.bfloat16)
    picked = jnp.dot(
        chooser,
        jnp.concatenate([high.astype(jnp.bfloat16), low], axis=0),
        preferred_element_type=jnp.float32,
    )
    residual_vectors = (recv_x.astype(jnp.float32) - picked).astype(jnp.bfloat16)
    residual_vectors = jnp.where(valid[:, None], residual_vectors, jnp.zeros_like(residual_vectors))
    routed = jnp.dot(
        residual_vectors, orthogonal_quantizer_turn, preferred_element_type=jnp.float32
    ).astype(jnp.bfloat16)
    return (routed, new_centroids)


def solution(mesh):
    return jax.shard_map(
        shards,
        mesh=mesh,
        in_specs=(P(("rows", "owners"), None), P(), P(), P(("rows", "owners")), P(), P()),
        out_specs=(P(("rows", "owners"), None), P()),
        check_vma=False,
    )
```

```python
import jax
import jax.numpy as jnp
from jax import lax
from jax.sharding import PartitionSpec as P

CAP = 512


PRIOR = 32.0


def _ring(axis, shift):
    if axis == "y":
        return "rows", [(z * 4 + y, z * 4 + (y + shift) % 4) for z in range(4) for y in range(4)]
    if axis == "z":
        return "rows", [(z * 4 + y, ((z + shift) % 4) * 4 + y) for z in range(4) for y in range(4)]
    return "owners", [(x * 2 + c, ((x + shift) % 4) * 2 + c) for x in range(4) for c in range(2)]


def _place(axis):
    if axis == "y":
        return lax.axis_index("rows") % 4
    if axis == "z":
        return lax.axis_index("rows") // 4
    return lax.axis_index("owners") // 2


_CORES = [(s, s ^ 1) for s in range(8)]


def _scatter_sum(d, axis):
    if axis == "core":
        me = lax.axis_index("owners") % 2
        halves = d.reshape(2, d.shape[0] // 2, d.shape[1])
        mine = lax.dynamic_index_in_dim(halves, me, 0, keepdims=False)
        other = lax.dynamic_index_in_dim(halves, 1 - me, 0, keepdims=False)
        return mine + lax.ppermute(other, "owners", _CORES)
    me = _place(axis)
    pieces = d.reshape(4, d.shape[0] // 4, d.shape[1])
    acc = lax.dynamic_index_in_dim(pieces, me, 0, keepdims=False)
    for shift in (1, 2, 3):
        name, perm = _ring(axis, shift)
        piece = lax.dynamic_index_in_dim(pieces, (me + shift) % 4, 0, keepdims=False)
        acc = acc + lax.ppermute(piece, name, perm)
    return acc


def _gather(d, axis):
    if axis == "core":
        me = lax.axis_index("owners") % 2
        out = jnp.zeros((2,) + d.shape, d.dtype)
        out = lax.dynamic_update_index_in_dim(out, d, me, 0)
        out = lax.dynamic_update_index_in_dim(out, lax.ppermute(d, "owners", _CORES), 1 - me, 0)
        return out.reshape(2 * d.shape[0], d.shape[1])
    me = _place(axis)
    out = jnp.zeros((4,) + d.shape, d.dtype)
    out = lax.dynamic_update_index_in_dim(out, d, me, 0)
    for shift in (1, 2, 3):
        name, perm = _ring(axis, shift)
        out = lax.dynamic_update_index_in_dim(out, lax.ppermute(d, name, perm), (me - shift) % 4, 0)
    return out.reshape(4 * d.shape[0], d.shape[1])


def _all_sum(d):
    order = ("core", "y", "z", "x")
    for axis in order:
        d = _scatter_sum(d, axis)
    for axis in reversed(order):
        d = _gather(d, axis)
    return d


def shards(
    instrument_feature_matrix,
    partition_prototypes,
    softmax_sharpness_divisor,
    chosen_partition_label,
    partition_holder_team,
    orthogonal_quantizer_turn,
):
    groups = lax.axis_size("owners")
    clusters, width = partition_prototypes.shape
    rows = instrument_feature_matrix.shape[0]
    x = instrument_feature_matrix
    labels = chosen_partition_label

    cent_bf = partition_prototypes.astype(jnp.bfloat16)
    prototype_length_squared_term = jnp.sum(partition_prototypes * partition_prototypes, axis=1)
    pairwise_dot_matrix = jnp.dot(x, cent_bf.T, preferred_element_type=jnp.float32)
    partition_affinity_logits = (
        2.0 * pairwise_dot_matrix - prototype_length_squared_term[None, :]
    ) / softmax_sharpness_divisor[0]
    weights = jax.nn.softmax(partition_affinity_logits, axis=1)
    weights_bf = weights.astype(jnp.bfloat16)
    part_counts = jnp.sum(weights, axis=0)
    pad = (-(clusters + 1)) % 128 + 1
    weights_wide = jnp.pad(weights_bf, ((0, 0), (0, pad)))
    packed = lax.dot_general(
        weights_wide, x, (((0,), (0,)), ((), ())), preferred_element_type=jnp.float32
    )
    packed = lax.dynamic_update_slice(packed, part_counts.reshape(1, width), (clusters, 0))
    total = _all_sum(packed)

    every_x = lax.all_gather(x, "owners", axis=0, tiled=False)
    every_label = lax.all_gather(labels, "owners", axis=0, tiled=False)
    me = lax.axis_index("owners")
    mine = jnp.take(partition_holder_team, every_label, axis=0, mode="clip") == me
    mine_i = mine.astype(jnp.int32)
    rank_in_group = jnp.cumsum(mine_i, axis=1) - mine_i
    sources = jnp.broadcast_to(jnp.arange(groups, dtype=jnp.int32)[:, None], mine.shape)
    slot_index = jnp.where(mine, sources * CAP + rank_in_group, groups * CAP)
    row_of = jnp.broadcast_to(jnp.arange(rows, dtype=jnp.int32)[None, :], mine.shape) + sources * rows
    source_row = jnp.zeros((groups * CAP,), jnp.int32).at[slot_index.reshape(-1)].set(
        row_of.reshape(-1), mode="drop"
    )
    recv_label = jnp.full((groups * CAP,), -1, jnp.int32).at[slot_index.reshape(-1)].set(
        every_label.reshape(-1), mode="drop"
    )
    recv_x = jnp.take(every_x.reshape(groups * rows, width), source_row, axis=0, mode="clip")

    valid = recv_label >= 0
    chooser = (recv_label[:, None] == jnp.arange(clusters, dtype=jnp.int32)[None, :]).astype(
        jnp.bfloat16
    )
    chooser = jnp.concatenate([chooser, chooser], axis=1)

    total_sums = total[:clusters]
    total_counts = total[clusters]
    new_centroids = (total_sums + PRIOR * partition_prototypes) * (
        1.0 / (total_counts + PRIOR)
    )[:, None]
    high = lax.reduce_precision(new_centroids, exponent_bits=8, mantissa_bits=7)
    low = (new_centroids - high).astype(jnp.bfloat16)
    picked = jnp.dot(
        chooser,
        jnp.concatenate([high.astype(jnp.bfloat16), low], axis=0),
        preferred_element_type=jnp.float32,
    )
    residual_vectors = (recv_x.astype(jnp.float32) - picked).astype(jnp.bfloat16)
    residual_vectors = jnp.where(valid[:, None], residual_vectors, jnp.zeros_like(residual_vectors))
    routed = jnp.dot(
        residual_vectors, orthogonal_quantizer_turn, preferred_element_type=jnp.float32
    ).astype(jnp.bfloat16)
    return (routed, new_centroids)


def solution(mesh):
    return jax.shard_map(
        shards,
        mesh=mesh,
        in_specs=(P(("rows", "owners"), None), P(), P(), P(("rows", "owners")), P(), P()),
        out_specs=(P(("rows", "owners"), None), P()),
        check_vma=False,
    )
```

```python
import jax
import jax.numpy as jnp
from jax import lax
from jax.sharding import PartitionSpec as P

CAP = 512


PRIOR = 32.0


def _ring(axis, shift):
    if axis == "y":
        return "rows", [(z * 4 + y, z * 4 + (y + shift) % 4) for z in range(4) for y in range(4)]
    if axis == "z":
        return "rows", [(z * 4 + y, ((z + shift) % 4) * 4 + y) for z in range(4) for y in range(4)]
    return "owners", [(x * 2 + c, ((x + shift) % 4) * 2 + c) for x in range(4) for c in range(2)]


def _place(axis):
    if axis == "y":
        return lax.axis_index("rows") % 4
    if axis == "z":
        return lax.axis_index("rows") // 4
    return lax.axis_index("owners") // 2


_CORES = [(s, s ^ 1) for s in range(8)]


def _scatter_sum(d, axis):
    if axis == "core":
        me = lax.axis_index("owners") % 2
        halves = d.reshape(2, d.shape[0] // 2, d.shape[1])
        mine = lax.dynamic_index_in_dim(halves, me, 0, keepdims=False)
        other = lax.dynamic_index_in_dim(halves, 1 - me, 0, keepdims=False)
        return mine + lax.ppermute(other, "owners", _CORES)
    me = _place(axis)
    pieces = d.reshape(4, d.shape[0] // 4, d.shape[1])
    acc = lax.dynamic_index_in_dim(pieces, me, 0, keepdims=False)
    for shift in (1, 2, 3):
        name, perm = _ring(axis, shift)
        piece = lax.dynamic_index_in_dim(pieces, (me + shift) % 4, 0, keepdims=False)
        acc = acc + lax.ppermute(piece, name, perm)
    return acc


def _gather(d, axis):
    if axis == "core":
        me = lax.axis_index("owners") % 2
        out = jnp.zeros((2,) + d.shape, d.dtype)
        out = lax.dynamic_update_index_in_dim(out, d, me, 0)
        out = lax.dynamic_update_index_in_dim(out, lax.ppermute(d, "owners", _CORES), 1 - me, 0)
        return out.reshape(2 * d.shape[0], d.shape[1])
    me = _place(axis)
    out = jnp.zeros((4,) + d.shape, d.dtype)
    out = lax.dynamic_update_index_in_dim(out, d, me, 0)
    for shift in (1, 2, 3):
        name, perm = _ring(axis, shift)
        out = lax.dynamic_update_index_in_dim(out, lax.ppermute(d, name, perm), (me - shift) % 4, 0)
    return out.reshape(4 * d.shape[0], d.shape[1])


def _all_sum(d):
    order = ("core", "y", "z", "x")
    for axis in order:
        d = _scatter_sum(d, axis)
    for axis in reversed(order):
        d = _gather(d, axis)
    return d


def shards(
    instrument_feature_matrix,
    partition_prototypes,
    softmax_sharpness_divisor,
    chosen_partition_label,
    partition_holder_team,
    orthogonal_quantizer_turn,
):
    groups = lax.axis_size("owners")
    clusters, width = partition_prototypes.shape
    rows = instrument_feature_matrix.shape[0]
    x = instrument_feature_matrix
    labels = chosen_partition_label

    cent_bf = partition_prototypes.astype(jnp.bfloat16)
    prototype_length_squared_term = jnp.sum(partition_prototypes * partition_prototypes, axis=1)
    pairwise_dot_matrix = jnp.dot(x, cent_bf.T, preferred_element_type=jnp.float32)
    partition_affinity_logits = (
        2.0 * pairwise_dot_matrix - prototype_length_squared_term[None, :]
    ) / softmax_sharpness_divisor[0]
    weights = jax.nn.softmax(partition_affinity_logits, axis=1)
    weights_bf = weights.astype(jnp.bfloat16)
    part_counts = jnp.sum(weights, axis=0)
    pad = (-(clusters + 1)) % 128 + 1
    weights_wide = jnp.pad(weights_bf, ((0, 0), (0, pad)))
    packed = lax.dot_general(
        weights_wide, x, (((0,), (0,)), ((), ())), preferred_element_type=jnp.float32
    )
    packed = lax.dynamic_update_slice(packed, part_counts.reshape(1, width), (clusters, 0))
    total = _all_sum(packed)

    every_x = lax.all_gather(x, "owners", axis=0, tiled=True)
    owner_group = jnp.take(partition_holder_team, labels, axis=0, mode="clip")
    onehot = (owner_group[:, None] == jnp.arange(groups, dtype=jnp.int32)[None, :]).astype(jnp.int32)
    before = jnp.cumsum(onehot, axis=0) - onehot
    rank_in_group = jnp.sum(before * onehot, axis=1)
    slot_index = owner_group * CAP + rank_in_group
    source_row = (
        jnp.zeros((groups * CAP,), jnp.int32).at[slot_index].set(jnp.arange(rows, dtype=jnp.int32))
    )
    slot_label = jnp.full((groups * CAP,), -1, jnp.int32).at[slot_index].set(labels)
    tables = jnp.stack([source_row.reshape(groups, CAP), slot_label.reshape(groups, CAP)], axis=1)
    tables = lax.all_to_all(tables, "owners", split_axis=0, concat_axis=0, tiled=True)
    sender = jnp.arange(groups, dtype=jnp.int32)[:, None] * rows
    recv_row = (tables[:, 0] + sender).reshape(groups * CAP)
    recv_label = tables[:, 1].reshape(groups * CAP)
    recv_x = jnp.take(every_x, recv_row, axis=0, mode="clip")

    valid = recv_label >= 0
    chooser = (recv_label[:, None] == jnp.arange(clusters, dtype=jnp.int32)[None, :]).astype(
        jnp.bfloat16
    )
    chooser = jnp.concatenate([chooser, chooser], axis=1)

    total_sums = total[:clusters]
    total_counts = total[clusters]
    new_centroids = (total_sums + PRIOR * partition_prototypes) * (
        1.0 / (total_counts + PRIOR)
    )[:, None]
    high = lax.reduce_precision(new_centroids, exponent_bits=8, mantissa_bits=7)
    low = (new_centroids - high).astype(jnp.bfloat16)
    picked = jnp.dot(
        chooser,
        jnp.concatenate([high.astype(jnp.bfloat16), low], axis=0),
        preferred_element_type=jnp.float32,
    )
    residual_vectors = (recv_x.astype(jnp.float32) - picked).astype(jnp.bfloat16)
    residual_vectors = jnp.where(valid[:, None], residual_vectors, jnp.zeros_like(residual_vectors))
    routed = jnp.dot(
        residual_vectors, orthogonal_quantizer_turn, preferred_element_type=jnp.float32
    ).astype(jnp.bfloat16)
    return (routed, new_centroids)


def solution(mesh):
    return jax.shard_map(
        shards,
        mesh=mesh,
        in_specs=(P(("rows", "owners"), None), P(), P(), P(("rows", "owners")), P(), P()),
        out_specs=(P(("rows", "owners"), None), P()),
        check_vma=False,
    )
```

```python
import jax
import jax.numpy as jnp
from jax import lax
from jax.sharding import PartitionSpec as P

CAP = 512


PRIOR = 32.0


def _ring(axis, shift):
    if axis == "y":
        return "rows", [(z * 4 + y, z * 4 + (y + shift) % 4) for z in range(4) for y in range(4)]
    if axis == "z":
        return "rows", [(z * 4 + y, ((z + shift) % 4) * 4 + y) for z in range(4) for y in range(4)]
    return "owners", [(x * 2 + c, ((x + shift) % 4) * 2 + c) for x in range(4) for c in range(2)]


def _place(axis):
    if axis == "y":
        return lax.axis_index("rows") % 4
    if axis == "z":
        return lax.axis_index("rows") // 4
    return lax.axis_index("owners") // 2


_CORES = [(s, s ^ 1) for s in range(8)]


def _scatter_sum(d, axis):
    if axis == "core":
        me = lax.axis_index("owners") % 2
        halves = d.reshape(2, d.shape[0] // 2, d.shape[1])
        mine = lax.dynamic_index_in_dim(halves, me, 0, keepdims=False)
        other = lax.dynamic_index_in_dim(halves, 1 - me, 0, keepdims=False)
        return mine + lax.ppermute(other, "owners", _CORES)
    me = _place(axis)
    pieces = d.reshape(4, d.shape[0] // 4, d.shape[1])
    acc = lax.dynamic_index_in_dim(pieces, me, 0, keepdims=False)
    for shift in (1, 2, 3):
        name, perm = _ring(axis, shift)
        piece = lax.dynamic_index_in_dim(pieces, (me + shift) % 4, 0, keepdims=False)
        acc = acc + lax.ppermute(piece, name, perm)
    return acc


def _gather(d, axis):
    if axis == "core":
        me = lax.axis_index("owners") % 2
        out = jnp.zeros((2,) + d.shape, d.dtype)
        out = lax.dynamic_update_index_in_dim(out, d, me, 0)
        out = lax.dynamic_update_index_in_dim(out, lax.ppermute(d, "owners", _CORES), 1 - me, 0)
        return out.reshape(2 * d.shape[0], d.shape[1])
    me = _place(axis)
    out = jnp.zeros((4,) + d.shape, d.dtype)
    out = lax.dynamic_update_index_in_dim(out, d, me, 0)
    for shift in (1, 2, 3):
        name, perm = _ring(axis, shift)
        out = lax.dynamic_update_index_in_dim(out, lax.ppermute(d, name, perm), (me - shift) % 4, 0)
    return out.reshape(4 * d.shape[0], d.shape[1])


def _all_sum(d):
    order = ("core", "y", "z", "x")
    for axis in order:
        d = _scatter_sum(d, axis)
    for axis in reversed(order):
        d = _gather(d, axis)
    return d


def shards(
    instrument_feature_matrix,
    partition_prototypes,
    softmax_sharpness_divisor,
    chosen_partition_label,
    partition_holder_team,
    orthogonal_quantizer_turn,
):
    groups = lax.axis_size("owners")
    clusters, width = partition_prototypes.shape
    rows = instrument_feature_matrix.shape[0]
    x = instrument_feature_matrix
    labels = chosen_partition_label

    cent_bf = partition_prototypes.astype(jnp.bfloat16)
    prototype_length_squared_term = jnp.sum(partition_prototypes * partition_prototypes, axis=1)
    pairwise_dot_matrix = jnp.dot(x, cent_bf.T, preferred_element_type=jnp.float32)
    partition_affinity_logits = (
        2.0 * pairwise_dot_matrix - prototype_length_squared_term[None, :]
    ) / softmax_sharpness_divisor[0]
    weights = jax.nn.softmax(partition_affinity_logits, axis=1)
    weights_bf = weights.astype(jnp.bfloat16)
    part_counts = jnp.sum(weights, axis=0)
    pad = (-(clusters + 1)) % 128 + 1
    weights_wide = jnp.pad(weights_bf, ((0, 0), (0, pad)))
    packed = lax.dot_general(
        weights_wide, x, (((0,), (0,)), ((), ())), preferred_element_type=jnp.float32
    )
    packed = lax.dynamic_update_slice(packed, part_counts.reshape(1, width), (clusters, 0))
    partial = packed
    for axis in ("core", "y", "z", "x"):
        partial = _scatter_sum(partial, axis)
    partial = _gather(partial, "x")
    partial = _gather(partial, "z")

    every_x = lax.all_gather(x, "owners", axis=0, tiled=False)
    owner_group = jnp.take(partition_holder_team, labels, axis=0, mode="clip")
    onehot = (owner_group[:, None] == jnp.arange(groups, dtype=jnp.int32)[None, :]).astype(jnp.int32)
    before = jnp.cumsum(onehot, axis=0) - onehot
    rank_in_group = jnp.sum(before * onehot, axis=1)
    slot_index = owner_group * CAP + rank_in_group
    source_row = (
        jnp.zeros((groups * CAP,), jnp.int32).at[slot_index].set(jnp.arange(rows, dtype=jnp.int32))
    )
    slot_label = jnp.full((groups * CAP,), -1, jnp.int32).at[slot_index].set(labels)
    tables = jnp.stack([source_row.reshape(groups, CAP), slot_label.reshape(groups, CAP)], axis=1)
    tables = lax.all_to_all(tables, "owners", split_axis=0, concat_axis=0, tiled=True)
    recv_label = tables[:, 1].reshape(groups * CAP)
    picker = (tables[:, 0][:, :, None] == jnp.arange(rows, dtype=jnp.int32)[None, None, :]).astype(
        jnp.bfloat16
    )
    recv_x = jnp.einsum(
        "sqn,snd->sqd", picker, every_x, preferred_element_type=jnp.float32
    ).astype(jnp.bfloat16).reshape(groups * CAP, width)
    partial, recv_x = lax.optimization_barrier((partial, recv_x))
    for axis in ("y", "core"):
        partial = _gather(partial, axis)
    total = partial

    valid = recv_label >= 0
    chooser = (recv_label[:, None] == jnp.arange(clusters, dtype=jnp.int32)[None, :]).astype(
        jnp.bfloat16
    )
    chooser = jnp.concatenate([chooser, chooser], axis=1)

    total_sums = total[:clusters]
    total_counts = total[clusters]
    new_centroids = (total_sums + PRIOR * partition_prototypes) * (
        1.0 / (total_counts + PRIOR)
    )[:, None]
    high = lax.reduce_precision(new_centroids, exponent_bits=8, mantissa_bits=7)
    low = (new_centroids - high).astype(jnp.bfloat16)
    picked = jnp.dot(
        chooser,
        jnp.concatenate([high.astype(jnp.bfloat16), low], axis=0),
        preferred_element_type=jnp.float32,
    )
    residual_vectors = (recv_x.astype(jnp.float32) - picked).astype(jnp.bfloat16)
    residual_vectors = jnp.where(valid[:, None], residual_vectors, jnp.zeros_like(residual_vectors))
    routed = jnp.dot(
        residual_vectors, orthogonal_quantizer_turn, preferred_element_type=jnp.float32
    ).astype(jnp.bfloat16)
    return (routed, new_centroids)


def solution(mesh):
    return jax.shard_map(
        shards,
        mesh=mesh,
        in_specs=(P(("rows", "owners"), None), P(), P(), P(("rows", "owners")), P(), P()),
        out_specs=(P(("rows", "owners"), None), P()),
        check_vma=False,
    )
```

```python
import jax
import jax.numpy as jnp
from jax import lax
from jax.sharding import PartitionSpec as P

CAP = 512


PRIOR = 32.0


def _ring(axis, shift):
    if axis == "y":
        return "rows", [(z * 4 + y, z * 4 + (y + shift) % 4) for z in range(4) for y in range(4)]
    if axis == "z":
        return "rows", [(z * 4 + y, ((z + shift) % 4) * 4 + y) for z in range(4) for y in range(4)]
    return "owners", [(x * 2 + c, ((x + shift) % 4) * 2 + c) for x in range(4) for c in range(2)]


def _place(axis):
    if axis == "y":
        return lax.axis_index("rows") % 4
    if axis == "z":
        return lax.axis_index("rows") // 4
    return lax.axis_index("owners") // 2


_CORES = [(s, s ^ 1) for s in range(8)]


def _scatter_sum(d, axis):
    if axis == "core":
        me = lax.axis_index("owners") % 2
        halves = d.reshape(2, d.shape[0] // 2, d.shape[1])
        mine = lax.dynamic_index_in_dim(halves, me, 0, keepdims=False)
        other = lax.dynamic_index_in_dim(halves, 1 - me, 0, keepdims=False)
        return mine + lax.ppermute(other, "owners", _CORES)
    me = _place(axis)
    pieces = d.reshape(4, d.shape[0] // 4, d.shape[1])
    acc = lax.dynamic_index_in_dim(pieces, me, 0, keepdims=False)
    for shift in (1, 2, 3):
        name, perm = _ring(axis, shift)
        piece = lax.dynamic_index_in_dim(pieces, (me + shift) % 4, 0, keepdims=False)
        acc = acc + lax.ppermute(piece, name, perm)
    return acc


def _gather(d, axis):
    if axis == "core":
        me = lax.axis_index("owners") % 2
        out = jnp.zeros((2,) + d.shape, d.dtype)
        out = lax.dynamic_update_index_in_dim(out, d, me, 0)
        out = lax.dynamic_update_index_in_dim(out, lax.ppermute(d, "owners", _CORES), 1 - me, 0)
        return out.reshape(2 * d.shape[0], d.shape[1])
    me = _place(axis)
    out = jnp.zeros((4,) + d.shape, d.dtype)
    out = lax.dynamic_update_index_in_dim(out, d, me, 0)
    for shift in (1, 2, 3):
        name, perm = _ring(axis, shift)
        out = lax.dynamic_update_index_in_dim(out, lax.ppermute(d, name, perm), (me - shift) % 4, 0)
    return out.reshape(4 * d.shape[0], d.shape[1])


def _all_sum(d):
    order = ("core", "y", "z", "x")
    for axis in order:
        d = _scatter_sum(d, axis)
    for axis in reversed(order):
        d = _gather(d, axis)
    return d


def shards(
    instrument_feature_matrix,
    partition_prototypes,
    softmax_sharpness_divisor,
    chosen_partition_label,
    partition_holder_team,
    orthogonal_quantizer_turn,
):
    groups = lax.axis_size("owners")
    clusters, width = partition_prototypes.shape
    rows = instrument_feature_matrix.shape[0]
    x = instrument_feature_matrix
    labels = chosen_partition_label

    cent_bf = partition_prototypes.astype(jnp.bfloat16)
    prototype_length_squared_term = jnp.sum(partition_prototypes * partition_prototypes, axis=1)
    pairwise_dot_matrix = jnp.dot(x, cent_bf.T, preferred_element_type=jnp.float32)
    partition_affinity_logits = (
        2.0 * pairwise_dot_matrix - prototype_length_squared_term[None, :]
    ) / softmax_sharpness_divisor[0]
    weights = jax.nn.softmax(partition_affinity_logits, axis=1)
    weights_bf = weights.astype(jnp.bfloat16)
    part_counts = jnp.sum(weights, axis=0)
    pad = (-(clusters + 1)) % 128 + 1
    weights_wide = jnp.pad(weights_bf, ((0, 0), (0, pad)))
    packed = lax.dot_general(
        weights_wide, x, (((0,), (0,)), ((), ())), preferred_element_type=jnp.float32
    )
    packed = lax.dynamic_update_slice(packed, part_counts.reshape(1, width), (clusters, 0))
    partial = packed
    for axis in ("core", "y", "z", "x"):
        partial = _scatter_sum(partial, axis)
    partial = _gather(partial, "x")
    partial = _gather(partial, "z")

    every_x = lax.all_gather(x, "owners", axis=0, tiled=False)
    owner_group = jnp.take(partition_holder_team, labels, axis=0, mode="clip")
    onehot = (owner_group[:, None] == jnp.arange(groups, dtype=jnp.int32)[None, :]).astype(jnp.int32)
    before = jnp.cumsum(onehot, axis=0) - onehot
    rank_in_group = jnp.sum(before * onehot, axis=1)
    slot_index = owner_group * CAP + rank_in_group
    source_row = (
        jnp.zeros((groups * CAP,), jnp.int32).at[slot_index].set(jnp.arange(rows, dtype=jnp.int32))
    )
    slot_label = jnp.full((groups * CAP,), -1, jnp.int32).at[slot_index].set(labels)
    tables = jnp.stack([source_row.reshape(groups, CAP), slot_label.reshape(groups, CAP)], axis=1)
    tables = lax.all_to_all(tables, "owners", split_axis=0, concat_axis=0, tiled=True)
    recv_label = tables[:, 1].reshape(groups * CAP)
    picker = (tables[:, 0][:, :, None] == jnp.arange(rows, dtype=jnp.int32)[None, None, :]).astype(
        jnp.bfloat16
    )
    recv_x = jnp.einsum(
        "sqn,snd->sqd", picker, every_x, preferred_element_type=jnp.float32
    ).astype(jnp.bfloat16).reshape(groups * CAP, width)

    valid = recv_label >= 0
    chooser = (recv_label[:, None] == jnp.arange(clusters, dtype=jnp.int32)[None, :]).astype(
        jnp.bfloat16
    )
    chooser = jnp.concatenate([chooser, chooser], axis=1)
    partial = _gather(partial, "y")
    partial, recv_x, chooser = lax.optimization_barrier((partial, recv_x, chooser))
    partial = _gather(partial, "core")
    total = partial

    total_sums = total[:clusters]
    total_counts = total[clusters]
    new_centroids = (total_sums + PRIOR * partition_prototypes) * (
        1.0 / (total_counts + PRIOR)
    )[:, None]
    high = lax.reduce_precision(new_centroids, exponent_bits=8, mantissa_bits=7)
    low = (new_centroids - high).astype(jnp.bfloat16)
    picked = jnp.dot(
        chooser,
        jnp.concatenate([high.astype(jnp.bfloat16), low], axis=0),
        preferred_element_type=jnp.float32,
    )
    residual_vectors = (recv_x.astype(jnp.float32) - picked).astype(jnp.bfloat16)
    residual_vectors = jnp.where(valid[:, None], residual_vectors, jnp.zeros_like(residual_vectors))
    routed = jnp.dot(
        residual_vectors, orthogonal_quantizer_turn, preferred_element_type=jnp.float32
    ).astype(jnp.bfloat16)
    return (routed, new_centroids)


def solution(mesh):
    return jax.shard_map(
        shards,
        mesh=mesh,
        in_specs=(P(("rows", "owners"), None), P(), P(), P(("rows", "owners")), P(), P()),
        out_specs=(P(("rows", "owners"), None), P()),
        check_vma=False,
    )
```
